128 devices in a mesh: prow: 8 (over x, core), pcol: 16 (over y, z).
Axes of the slice: x: 4, y: 4, z: 4, core: 2. Of those that a mesh axis runs over, the one named last changes fastest.
Arguments:
- basis: bfloat16 [512, 256], replicated, may hold values from -0.25 to 0.25
- potentials: float32 [8, 512], replicated, may hold values from -6 to 6
- orbitals: bfloat16 [64, 512], P('pcol'), may hold values from -6 to 6
- chan_orbital: int32 [256], replicated, may hold values from 0 to 63
- pair_list: int32 [24576, 3], P(('prow', 'pcol')), may hold values from 0 to 255, as said below
- slot_list: int32 [24576], P(('prow', 'pcol')), may hold values from 0 to 255
- coefs: float32 [24576, 2], P(('prow', 'pcol')), may hold values from -6 to 6
- exchange_ops: bfloat16 [24576, 128, 256], P(('prow', 'pcol')), may hold values from -1.1953125 to 1.1953125
Outputs:
- hamiltonian: bfloat16 [32, 8, 2, 16, 256, 256], P(None, 'prow', None, 'pcol')
The draws below stay inside these ranges and needn't reach their ends.
Inputs may be any that keep to these rules, and one draw needn't show every extreme that they name: `pair_list`: columns 0 and 1 are channels a, b; column 2 is a multipole order below 8. (b // 16 - a // 16) modulo 256 // 16 is below 2. Terms of one device with the same slot s have the same two channels, and the block (a, b) belongs to owner s // 2 in prow-major order: a % 8 and b % 16 are that owner's prow and pcol indices.
All inputs are finite; a program needn't handle non-finite values.
Results may differ from the reference program's by a relative error of at most 0.0058.
Values may be sent and summed in bfloat16 or wider, within the bound.
No kernel may reach another device: no remote copies, remote signals or barrier semaphores. Data moves between devices by JAX's collectives and lax.ppermute only.
A program may use at most 320 MiB of HBM per device.

```python
import jax
import jax.numpy as jnp
from jax import lax

NB = 256
NQ = 512
NQX = 128
NORB = 64
LAM = 8
CAP = 2
BAND = 2
RBLK = 32
EDEV = 192
CHAN = 256
SLOTS = 256
ENTRIES = 24576
N_PROW = 8
N_PCOL = 16
DEVICES = 128


def common_lists(key):
    order_key = jax.random.fold_in(key, 11)
    block_key = jax.random.fold_in(key, 23)
    multipole_key = jax.random.fold_in(key, 37)
    repeat_key = jax.random.fold_in(key, 41)
    device_keys = jax.random.split(order_key, DEVICES)
    slot_orders = jax.vmap(lambda device_key: jax.random.permutation(device_key, SLOTS))(device_keys).astype(jnp.int32)
    distinct = min(EDEV * 2 // 3, SLOTS)
    term_range = jnp.arange(EDEV, dtype=jnp.int32)
    repeats = jax.random.randint(repeat_key, (DEVICES, EDEV), 0, distinct, dtype=jnp.int32)
    positions = jnp.where(term_range[None, :] < distinct, term_range[None, :], repeats).astype(jnp.int32)
    slot_table = jnp.take_along_axis(slot_orders, positions, axis=1)
    slot_table = slot_table.at[:, EDEV - 1].set(SLOTS - 1)
    block_table = jax.random.randint(block_key, (DEVICES, SLOTS), 0, RBLK * BAND, dtype=jnp.int32)
    chosen = jnp.take_along_axis(block_table, slot_table, axis=1)
    owner_index = slot_table // CAP
    owner_row = owner_index // N_PCOL
    owner_col = owner_index % N_PCOL
    col_groups = CHAN // N_PCOL
    first_chan = chosen // BAND * N_PROW + owner_row
    col_group = jnp.mod(first_chan // N_PCOL + chosen % BAND, col_groups)
    second_chan = col_group * N_PCOL + owner_col
    multipole = jax.random.randint(multipole_key, (DEVICES, EDEV), 0, LAM, dtype=jnp.int32)
    pair_rows = jnp.stack([first_chan, second_chan, multipole], axis=-1).reshape(ENTRIES, 3)
    return (pair_rows.astype(jnp.int32), slot_table.reshape(ENTRIES).astype(jnp.int32))


def draw_pair_list(key, part):
    return common_lists(key)[0]


def draw_slot_list(key, part):
    return common_lists(key)[1]


def set_ends(values, stream_key, smallest, high):
    longest = values.shape.index(max(values.shape))
    spots = []
    for shift in (0, 1):
        where = [jax.random.randint(jax.random.fold_in(stream_key, axis), (), 0, length) for axis, length in enumerate(values.shape)]
        where[longest] = (where[longest] + shift) % values.shape[longest]
        spots.append(tuple(where))
    return values.at[spots[0]].set(smallest).at[spots[1]].set(high)


def shard_levels(key, dims, pieces, smallest, top_value):
    level = 1.0
    for dim, blocks in pieces:
        heights = jax.random.uniform(jax.random.fold_in(jax.random.fold_in(key, 6), dim), (blocks,), jnp.float32, smallest / len(pieces), top_value / len(pieces))
        level = level * jnp.repeat(jnp.exp(heights), dims[dim] // blocks).reshape((-1,) + (1,) * (len(dims) - 1 - dim))
    return level


def normal_values(key, dims, scale, reach, cuts=(), kind=jnp.bfloat16):
    array = scale * jax.random.normal(key, dims, jnp.float32)
    if cuts:
        array = array * shard_levels(key, dims, cuts, -0.22, 0.18)
    return jnp.clip(array, -reach, reach).astype(kind)


def setup_inputs(seed: int = 0) -> dict:
    key_list = jax.random.split(jax.random.key(seed), 9)
    return {
        "basis": normal_values(key_list[0], (NQ, NB), NQ ** -0.5, 0.25),
        "potentials": normal_values(key_list[1], (LAM, NQ), 1.0, 6.0, (), jnp.float32),
        "orbitals": normal_values(key_list[2], (NORB, NQ), 1.0, 6.0, ((0, 16),)),
        "chan_orbital": set_ends(jax.random.randint(key_list[3], (CHAN,), 0, NORB), jax.random.fold_in(key_list[3], 1), 0, NORB - 1).astype(jnp.int32),
        "pair_list": draw_pair_list(jax.random.fold_in(key_list[8], 71), 0),
        "slot_list": draw_slot_list(jax.random.fold_in(key_list[8], 71), 0),
        "coefs": normal_values(key_list[6], (ENTRIES, 2), 1.0, 6.0, ((0, 128),), jnp.float32),
        "exchange_ops": normal_values(key_list[7], (ENTRIES, NQX, NB), 0.2, 1.1953125, ((0, 128),)),
    }


def build_tiles(weights_group, exchange_group, basis):
    weights_group, exchange_group = lax.optimization_barrier((weights_group, exchange_group))
    basis_float = basis.astype(jnp.float32)
    scaled = (weights_group.astype(jnp.float32)[:, :, None] * basis_float[None]).astype(jnp.bfloat16)
    scaled = lax.optimization_barrier(scaled)
    inner_rows = basis_float[:exchange_group.shape[1]]
    local_part = jnp.einsum('qa,gqb->gab', basis_float, scaled.astype(jnp.float32))
    exchange_part = jnp.einsum('qa,gqb->gab', inner_rows, exchange_group.astype(jnp.float32))
    return (local_part + exchange_part).astype(jnp.bfloat16)


def reference(basis, potentials, orbitals, chan_orbital, pair_list, slot_list, coefs, exchange_ops):
    orb_float = orbitals.astype(jnp.float32)
    col_groups = CHAN // N_PCOL
    block_count = RBLK * BAND
    dropped = DEVICES * block_count

    def add_device(carried, device_index):
        first_term = (device_index * EDEV).astype(jnp.int32)
        pair_rows = lax.dynamic_slice_in_dim(pair_list, first_term, EDEV, 0)
        term_slots = lax.dynamic_slice_in_dim(slot_list, first_term, EDEV, 0)
        factors = lax.dynamic_slice_in_dim(coefs, first_term, EDEV, 0)
        operands = lax.dynamic_slice_in_dim(exchange_ops, first_term, EDEV, 0)
        first_chan = pair_rows[:, 0]
        second_chan = pair_rows[:, 1]
        multipole = pair_rows[:, 2]
        first_orb = chan_orbital[first_chan]
        second_orb = chan_orbital[second_chan]
        radial = factors[:, 0:1] * potentials[multipole] + factors[:, 1:2] * (orb_float[first_orb] * orb_float[second_orb])
        slot_weight = jax.ops.segment_sum(radial, term_slots, num_segments=SLOTS).astype(jnp.bfloat16)
        slot_exchange = jax.ops.segment_sum(operands.astype(jnp.float32), term_slots, num_segments=SLOTS).astype(jnp.bfloat16)
        offset = jnp.mod(second_chan // N_PCOL - first_chan // N_PCOL, col_groups)
        block_index = ((first_chan // N_PROW) * BAND + offset).astype(jnp.int32)
        slot_ids = jax.ops.segment_max(block_index, term_slots, num_segments=SLOTS)
        owner_index = jnp.arange(SLOTS, dtype=jnp.int32) // CAP
        global_ids = jnp.where(slot_ids >= 0, owner_index * block_count + slot_ids, dropped).astype(jnp.int32)
        built_tiles = build_tiles(slot_weight, slot_exchange, basis)
        carried = carried.at[global_ids].add(built_tiles.astype(jnp.float32), mode="drop")
        return carried, None

    zeros_start = jnp.zeros((DEVICES * block_count, NB, NB), jnp.float32)
    summed_blocks, unused = lax.scan(add_device, zeros_start, jnp.arange(DEVICES, dtype=jnp.int32))
    blocks = summed_blocks.astype(jnp.bfloat16).reshape(N_PROW, N_PCOL, RBLK, BAND, NB, NB)
    return jnp.transpose(blocks, (2, 0, 3, 1, 4, 5))
```

```python
import jax
import jax.numpy as jnp
from jax import lax
from jax.sharding import PartitionSpec as P

CAP = 2
BAND = 2
RBLK = 32


def split_bf16(values):
    high = values.astype(jnp.bfloat16)
    low = (values - high.astype(jnp.float32)).astype(jnp.bfloat16)
    return high, low


def on_device(basis, potentials, orbitals, chan_orbital, pair_list, slot_list, coefs, exchange_ops):
    all_orbitals = lax.all_gather(orbitals, "pcol", axis=0, tiled=True)
    row_devs = lax.axis_size("prow")
    col_devs = lax.axis_size("pcol")
    slot_count = row_devs * col_devs * CAP
    chan_count = chan_orbital.shape[0]
    orb_count = all_orbitals.shape[0]
    point_count = basis.shape[0]
    spline_count = basis.shape[1]
    inner_count = exchange_ops.shape[1]
    term_count = exchange_ops.shape[0]
    col_groups = chan_count // col_devs
    block_count = RBLK * BAND
    first_chan = pair_list[:, 0]
    second_chan = pair_list[:, 1]
    multipole = pair_list[:, 2]
    channels = jnp.arange(chan_count, dtype=jnp.int32)
    orb_ids = jnp.arange(orb_count, dtype=jnp.int32)
    first_orb = jnp.sum(
        jnp.where(first_chan[:, None] == channels[None, :], chan_orbital[None, :], 0), axis=1
    )
    second_orb = jnp.sum(
        jnp.where(second_chan[:, None] == channels[None, :], chan_orbital[None, :], 0), axis=1
    )
    first_rows = jnp.dot(
        (first_orb[:, None] == orb_ids[None, :]).astype(jnp.bfloat16),
        all_orbitals,
        preferred_element_type=jnp.float32,
    )
    second_rows = jnp.dot(
        (second_orb[:, None] == orb_ids[None, :]).astype(jnp.bfloat16),
        all_orbitals,
        preferred_element_type=jnp.float32,
    )
    pick_pot = (
        multipole[:, None] == jnp.arange(potentials.shape[0], dtype=jnp.int32)[None, :]
    ).astype(jnp.float32)
    pot_rows = jnp.dot(pick_pot, potentials, precision=lax.Precision.HIGHEST)
    radial = coefs[:, 0:1] * pot_rows + coefs[:, 1:2] * (first_rows * second_rows)
    matches = slot_list[None, :] == jnp.arange(slot_count, dtype=jnp.int32)[:, None]
    slot_weight = jnp.dot(
        matches.astype(jnp.float32), radial, precision=lax.Precision.HIGHEST
    ).astype(jnp.bfloat16)
    exchange_rows = exchange_ops.reshape(term_count, inner_count * spline_count)
    slot_exchange = jnp.dot(
        matches.astype(jnp.bfloat16), exchange_rows, preferred_element_type=jnp.float32
    ).astype(jnp.bfloat16)
    offset = jnp.mod(second_chan // col_devs - first_chan // col_devs, col_groups)
    block_index = first_chan // row_devs * BAND + offset
    slot_ids = jnp.max(jnp.where(matches, block_index[None, :], -1), axis=1)

    payload = inner_count * spline_count + point_count + 1
    width = -(-payload // 128) * 128
    packed = jnp.concatenate(
        [
            slot_exchange,
            slot_weight,
            slot_ids.astype(jnp.bfloat16)[:, None],
            jnp.zeros((slot_count, width - payload), jnp.bfloat16),
        ],
        axis=1,
    )
    received = lax.all_to_all(packed, ("prow", "pcol"), 0, 0, tiled=True)

    idents = received[:, payload - 1].astype(jnp.float32).astype(jnp.int32)
    select = (jnp.arange(block_count, dtype=jnp.int32)[:, None] == idents[None, :]).astype(
        jnp.bfloat16
    )
    summed = jnp.dot(select, received[:, : payload - 1], preferred_element_type=jnp.float32)
    exchange_sum = summed[:, : inner_count * spline_count].reshape(
        block_count, inner_count, spline_count
    )
    weight_sum = summed[:, inner_count * spline_count :]
    basis_float = basis.astype(jnp.float32)
    scaled_high, scaled_low = split_bf16(weight_sum[:, :, None] * basis_float[None])
    exchange_high, exchange_low = split_bf16(exchange_sum)
    inner_rows = basis[:inner_count]
    tiles = (
        jnp.einsum("qa,gqb->gab", basis, scaled_high, preferred_element_type=jnp.float32)
        + jnp.einsum("qa,gqb->gab", basis, scaled_low, preferred_element_type=jnp.float32)
        + jnp.einsum("qa,gqb->gab", inner_rows, exchange_high, preferred_element_type=jnp.float32)
        + jnp.einsum("qa,gqb->gab", inner_rows, exchange_low, preferred_element_type=jnp.float32)
    )
    return tiles.astype(jnp.bfloat16).reshape(RBLK, 1, BAND, 1, spline_count, spline_count)


def solution(mesh):
    placed = (
        P(),
        P(),
        P("pcol", None),
        P(),
        P(("prow", "pcol"), None),
        P(("prow", "pcol")),
        P(("prow", "pcol"), None),
        P(("prow", "pcol"), None, None),
    )
    return jax.shard_map(
        on_device,
        mesh=mesh,
        in_specs=placed,
        out_specs=P(None, "prow", None, "pcol", None, None),
        check_vma=False,
    )
```

```python
import jax
import jax.numpy as jnp
from jax import lax
from jax.experimental import pallas as pl
from jax.sharding import PartitionSpec as P

CAP = 2
BAND = 2
RBLK = 32


def split_bf16(values):
    high = values.astype(jnp.bfloat16)
    low = (values - high.astype(jnp.float32)).astype(jnp.bfloat16)
    return high, low


def tile_kernel(weight_ref, exchange_ref, basis_t_ref, basis_ref, inner_t_ref, out_ref):
    left = basis_t_ref[...].astype(jnp.float32) * weight_ref[0]
    left_high, left_low = split_bf16(left)
    basis = basis_ref[...]
    acc = jnp.dot(left_high, basis, preferred_element_type=jnp.float32)
    acc += jnp.dot(left_low, basis, preferred_element_type=jnp.float32)
    exchange_high, exchange_low = split_bf16(exchange_ref[0])
    inner_t = inner_t_ref[...]
    acc += jnp.dot(inner_t, exchange_high, preferred_element_type=jnp.float32)
    acc += jnp.dot(inner_t, exchange_low, preferred_element_type=jnp.float32)
    out_ref[0] = acc.astype(out_ref.dtype)


def build_blocks(weight_sum, exchange_sum, basis):
    block_count, point_count = weight_sum.shape
    inner_count, spline_count = exchange_sum.shape[1:]
    basis_t = basis.T
    inner_t = basis[:inner_count].T
    return pl.pallas_call(
        tile_kernel,
        grid=(block_count,),
        in_specs=[
            pl.BlockSpec((1, 1, point_count), lambda g: (g, 0, 0)),
            pl.BlockSpec((1, inner_count, spline_count), lambda g: (g, 0, 0)),
            pl.BlockSpec((spline_count, point_count), lambda g: (0, 0)),
            pl.BlockSpec((point_count, spline_count), lambda g: (0, 0)),
            pl.BlockSpec((spline_count, inner_count), lambda g: (0, 0)),
        ],
        out_specs=pl.BlockSpec((1, spline_count, spline_count), lambda g: (g, 0, 0)),
        out_shape=jax.ShapeDtypeStruct((block_count, spline_count, spline_count), jnp.bfloat16),
    )(weight_sum.reshape(block_count, 1, point_count), exchange_sum, basis_t, basis, inner_t)


def on_device(basis, potentials, orbitals, chan_orbital, pair_list, slot_list, coefs, exchange_ops):
    row_devs = lax.axis_size("prow")
    col_devs = lax.axis_size("pcol")
    slot_count = row_devs * col_devs * CAP
    chan_count = chan_orbital.shape[0]
    point_count = basis.shape[0]
    spline_count = basis.shape[1]
    inner_count = exchange_ops.shape[1]
    col_groups = chan_count // col_devs
    block_count = RBLK * BAND
    first_chan = pair_list[:, 0]
    second_chan = pair_list[:, 1]
    multipole = pair_list[:, 2]
    matches = slot_list[None, :] == jnp.arange(slot_count, dtype=jnp.int32)[:, None]

    slot_exchange = jnp.einsum(
        "st,tqb->sqb",
        matches.astype(jnp.bfloat16),
        exchange_ops,
        preferred_element_type=jnp.float32,
    ).astype(jnp.bfloat16)
    received_exchange = lax.all_to_all(slot_exchange, ("prow", "pcol"), 0, 0, tiled=True)

    all_orbitals = lax.all_gather(orbitals, "pcol", axis=0, tiled=True)
    orb_count = all_orbitals.shape[0]
    channels = jnp.arange(chan_count, dtype=jnp.int32)
    orb_ids = jnp.arange(orb_count, dtype=jnp.int32)
    first_orb = jnp.sum(
        jnp.where(first_chan[:, None] == channels[None, :], chan_orbital[None, :], 0), axis=1
    )
    second_orb = jnp.sum(
        jnp.where(second_chan[:, None] == channels[None, :], chan_orbital[None, :], 0), axis=1
    )
    first_rows = jnp.dot(
        (first_orb[:, None] == orb_ids[None, :]).astype(jnp.bfloat16),
        all_orbitals,
        preferred_element_type=jnp.float32,
    )
    second_rows = jnp.dot(
        (second_orb[:, None] == orb_ids[None, :]).astype(jnp.bfloat16),
        all_orbitals,
        preferred_element_type=jnp.float32,
    )
    pick_pot = (
        multipole[:, None] == jnp.arange(potentials.shape[0], dtype=jnp.int32)[None, :]
    ).astype(jnp.float32)
    pot_rows = jnp.dot(pick_pot, potentials, precision=lax.Precision.HIGHEST)
    radial = coefs[:, 0:1] * pot_rows + coefs[:, 1:2] * (first_rows * second_rows)
    slot_weight = jnp.dot(
        matches.astype(jnp.float32), radial, precision=lax.Precision.HIGHEST
    ).astype(jnp.bfloat16)
    offset = jnp.mod(second_chan // col_devs - first_chan // col_devs, col_groups)
    block_index = first_chan // row_devs * BAND + offset
    slot_ids = jnp.max(jnp.where(matches, block_index[None, :], -1), axis=1)

    width = -(-(point_count + 1) // 128) * 128
    small = jnp.concatenate(
        [
            slot_weight,
            slot_ids.astype(jnp.bfloat16)[:, None],
            jnp.zeros((slot_count, width - point_count - 1), jnp.bfloat16),
        ],
        axis=1,
    )
    received_small = lax.all_to_all(small, ("prow", "pcol"), 0, 0, tiled=True)

    idents = received_small[:, point_count].astype(jnp.float32).astype(jnp.int32)
    select = (jnp.arange(block_count, dtype=jnp.int32)[:, None] == idents[None, :]).astype(
        jnp.bfloat16
    )
    weight_sum = jnp.dot(
        select, received_small[:, :point_count], preferred_element_type=jnp.float32
    )
    exchange_sum = jnp.einsum(
        "gs,sqb->gqb", select, received_exchange, preferred_element_type=jnp.float32
    )
    blocks = build_blocks(weight_sum, exchange_sum, basis)
    return blocks.reshape(RBLK, 1, BAND, 1, spline_count, spline_count)


def solution(mesh):
    placed = (
        P(),
        P(),
        P("pcol", None),
        P(),
        P(("prow", "pcol"), None),
        P(("prow", "pcol")),
        P(("prow", "pcol"), None),
        P(("prow", "pcol"), None, None),
    )
    return jax.shard_map(
        on_device,
        mesh=mesh,
        in_specs=placed,
        out_specs=P(None, "prow", None, "pcol", None, None),
        check_vma=False,
    )
```

```python
import jax
import jax.numpy as jnp
from jax import lax
from jax.experimental import pallas as pl
from jax.sharding import PartitionSpec as P

CAP = 2
BAND = 2
RBLK = 32


def split_bf16(values):
    high = values.astype(jnp.bfloat16)
    low = (values - high.astype(jnp.float32)).astype(jnp.bfloat16)
    return high, low


def tile_kernel(weight_ref, exchange_ref, basis_t_ref, basis_ref, inner_t_ref, out_ref):
    weight_col = jnp.broadcast_to(weight_ref[0], (8, weight_ref.shape[2])).T[:, 0:1]
    scaled = (weight_col * basis_ref[...].astype(jnp.float32)).astype(jnp.bfloat16)
    acc = jnp.dot(basis_t_ref[...], scaled, preferred_element_type=jnp.float32)
    exchange_high, exchange_low = split_bf16(exchange_ref[0])
    inner_t = inner_t_ref[...]
    acc += jnp.dot(inner_t, exchange_high, preferred_element_type=jnp.float32)
    acc += jnp.dot(inner_t, exchange_low, preferred_element_type=jnp.float32)
    out_ref[0] = acc.astype(out_ref.dtype)


def build_blocks(weight_sum, exchange_sum, basis):
    block_count, point_count = weight_sum.shape
    inner_count, spline_count = exchange_sum.shape[1:]
    basis_t = basis.T
    inner_t = basis[:inner_count].T
    return pl.pallas_call(
        tile_kernel,
        grid=(block_count,),
        in_specs=[
            pl.BlockSpec((1, 1, point_count), lambda g: (g, 0, 0)),
            pl.BlockSpec((1, inner_count, spline_count), lambda g: (g, 0, 0)),
            pl.BlockSpec((spline_count, point_count), lambda g: (0, 0)),
            pl.BlockSpec((point_count, spline_count), lambda g: (0, 0)),
            pl.BlockSpec((spline_count, inner_count), lambda g: (0, 0)),
        ],
        out_specs=pl.BlockSpec((1, spline_count, spline_count), lambda g: (g, 0, 0)),
        out_shape=jax.ShapeDtypeStruct((block_count, spline_count, spline_count), jnp.bfloat16),
    )(weight_sum.reshape(block_count, 1, point_count), exchange_sum, basis_t, basis, inner_t)


def on_device(basis, potentials, orbitals, chan_orbital, pair_list, slot_list, coefs, exchange_ops):
    row_devs = lax.axis_size("prow")
    col_devs = lax.axis_size("pcol")
    slot_count = row_devs * col_devs * CAP
    chan_count = chan_orbital.shape[0]
    point_count = basis.shape[0]
    spline_count = basis.shape[1]
    inner_count = exchange_ops.shape[1]
    col_groups = chan_count // col_devs
    block_count = RBLK * BAND
    first_chan = pair_list[:, 0]
    second_chan = pair_list[:, 1]
    multipole = pair_list[:, 2]
    matches = slot_list[None, :] == jnp.arange(slot_count, dtype=jnp.int32)[:, None]

    slot_exchange = jnp.einsum(
        "st,tqb->sqb",
        matches.astype(jnp.bfloat16),
        exchange_ops,
        preferred_element_type=jnp.float32,
    ).astype(jnp.bfloat16)
    received_exchange = lax.all_to_all(slot_exchange, ("prow", "pcol"), 0, 0, tiled=True)

    orb_local = orbitals.shape[0]
    orb_count = orb_local * col_devs
    placed_orbitals = lax.dynamic_update_slice_in_dim(
        jnp.zeros((orb_count, orbitals.shape[1]), orbitals.dtype),
        orbitals,
        lax.axis_index("pcol") * orb_local,
        0,
    )
    all_orbitals = lax.psum(placed_orbitals, "pcol")
    channels = jnp.arange(chan_count, dtype=jnp.int32)
    orb_ids = jnp.arange(orb_count, dtype=jnp.int32)
    first_orb = jnp.sum(
        jnp.where(first_chan[:, None] == channels[None, :], chan_orbital[None, :], 0), axis=1
    )
    second_orb = jnp.sum(
        jnp.where(second_chan[:, None] == channels[None, :], chan_orbital[None, :], 0), axis=1
    )
    first_rows = jnp.dot(
        (first_orb[:, None] == orb_ids[None, :]).astype(jnp.bfloat16),
        all_orbitals,
        preferred_element_type=jnp.float32,
    )
    second_rows = jnp.dot(
        (second_orb[:, None] == orb_ids[None, :]).astype(jnp.bfloat16),
        all_orbitals,
        preferred_element_type=jnp.float32,
    )
    pick_pot = (
        multipole[:, None] == jnp.arange(potentials.shape[0], dtype=jnp.int32)[None, :]
    ).astype(jnp.float32)
    pot_rows = jnp.dot(pick_pot, potentials, precision=lax.Precision.HIGHEST)
    radial = coefs[:, 0:1] * pot_rows + coefs[:, 1:2] * (first_rows * second_rows)
    slot_weight = jnp.dot(
        matches.astype(jnp.float32), radial, precision=lax.Precision.HIGHEST
    ).astype(jnp.bfloat16)
    offset = jnp.mod(second_chan // col_devs - first_chan // col_devs, col_groups)
    block_index = first_chan // row_devs * BAND + offset
    slot_ids = jnp.max(jnp.where(matches, block_index[None, :], -1), axis=1)

    width = -(-(point_count + 1) // 128) * 128
    small = jnp.concatenate(
        [
            slot_weight,
            slot_ids.astype(jnp.bfloat16)[:, None],
            jnp.zeros((slot_count, width - point_count - 1), jnp.bfloat16),
        ],
        axis=1,
    )
    received_small = lax.all_to_all(small, ("prow", "pcol"), 0, 0, tiled=True)

    idents = received_small[:, point_count].astype(jnp.float32).astype(jnp.int32)
    select = (jnp.arange(block_count, dtype=jnp.int32)[:, None] == idents[None, :]).astype(
        jnp.bfloat16
    )
    weight_sum = jnp.dot(
        select, received_small[:, :point_count], preferred_element_type=jnp.float32
    )
    exchange_sum = jnp.einsum(
        "gs,sqb->gqb", select, received_exchange, preferred_element_type=jnp.float32
    )
    blocks = build_blocks(weight_sum, exchange_sum, basis)
    return blocks.reshape(RBLK, 1, BAND, 1, spline_count, spline_count)


def solution(mesh):
    placed = (
        P(),
        P(),
        P("pcol", None),
        P(),
        P(("prow", "pcol"), None),
        P(("prow", "pcol")),
        P(("prow", "pcol"), None),
        P(("prow", "pcol"), None, None),
    )
    return jax.shard_map(
        on_device,
        mesh=mesh,
        in_specs=placed,
        out_specs=P(None, "prow", None, "pcol", None, None),
        check_vma=False,
    )
```

```python
import jax
import jax.numpy as jnp
from jax import lax
from jax.experimental import pallas as pl
from jax.sharding import PartitionSpec as P

CAP = 2
BAND = 2
RBLK = 32


def split_bf16(values):
    high = values.astype(jnp.bfloat16)
    low = (values - high.astype(jnp.float32)).astype(jnp.bfloat16)
    return high, low


def tile_kernel(weight_ref, exchange_ref, basis_t_ref, basis_ref, inner_t_ref, out_ref):
    basis_t = basis_t_ref[...]
    basis = basis_ref[...]
    inner_t = inner_t_ref[...]
    for j in range(out_ref.shape[0]):
        left = (basis_t * weight_ref[j : j + 1, :]).astype(jnp.bfloat16)
        acc = jnp.dot(left, basis, preferred_element_type=jnp.float32)
        exchange_high, exchange_low = split_bf16(exchange_ref[:, j, :])
        acc += jnp.dot(inner_t, exchange_high, preferred_element_type=jnp.float32)
        acc += jnp.dot(inner_t, exchange_low, preferred_element_type=jnp.float32)
        out_ref[j] = acc.astype(out_ref.dtype)


def build_blocks(weight_sum, exchange_sum, basis, group=8):
    block_count, point_count = weight_sum.shape
    inner_count, _, spline_count = exchange_sum.shape
    basis_t = basis.T.astype(jnp.float32)
    inner_t = basis[:inner_count].T
    return pl.pallas_call(
        tile_kernel,
        grid=(block_count // group,),
        in_specs=[
            pl.BlockSpec((group, point_count), lambda g: (g, 0)),
            pl.BlockSpec((inner_count, group, spline_count), lambda g: (0, g, 0)),
            pl.BlockSpec((spline_count, point_count), lambda g: (0, 0)),
            pl.BlockSpec((point_count, spline_count), lambda g: (0, 0)),
            pl.BlockSpec((spline_count, inner_count), lambda g: (0, 0)),
        ],
        out_specs=pl.BlockSpec((group, spline_count, spline_count), lambda g: (g, 0, 0)),
        out_shape=jax.ShapeDtypeStruct((block_count, spline_count, spline_count), jnp.bfloat16),
    )(weight_sum, exchange_sum, basis_t, basis, inner_t)


def on_device(basis, potentials, orbitals, chan_orbital, pair_list, slot_list, coefs, exchange_ops):
    row_devs = lax.axis_size("prow")
    col_devs = lax.axis_size("pcol")
    slot_count = row_devs * col_devs * CAP
    chan_count = chan_orbital.shape[0]
    point_count = basis.shape[0]
    spline_count = basis.shape[1]
    inner_count = exchange_ops.shape[1]
    col_groups = chan_count // col_devs
    block_count = RBLK * BAND
    first_chan = pair_list[:, 0]
    second_chan = pair_list[:, 1]
    multipole = pair_list[:, 2]
    matches = slot_list[None, :] == jnp.arange(slot_count, dtype=jnp.int32)[:, None]

    slot_exchange = jnp.einsum(
        "st,tqb->sqb",
        matches.astype(jnp.bfloat16),
        exchange_ops,
        preferred_element_type=jnp.float32,
    ).astype(jnp.bfloat16)
    received_exchange = lax.all_to_all(slot_exchange, ("prow", "pcol"), 0, 0, tiled=True)

    all_orbitals = lax.all_gather(orbitals, "pcol", axis=0, tiled=True)
    orb_count = all_orbitals.shape[0]
    channels = jnp.arange(chan_count, dtype=jnp.int32)
    orb_ids = jnp.arange(orb_count, dtype=jnp.int32)
    first_orb = jnp.sum(
        jnp.where(first_chan[:, None] == channels[None, :], chan_orbital[None, :], 0), axis=1
    )
    second_orb = jnp.sum(
        jnp.where(second_chan[:, None] == channels[None, :], chan_orbital[None, :], 0), axis=1
    )
    first_rows = jnp.dot(
        (first_orb[:, None] == orb_ids[None, :]).astype(jnp.bfloat16),
        all_orbitals,
        preferred_element_type=jnp.float32,
    )
    second_rows = jnp.dot(
        (second_orb[:, None] == orb_ids[None, :]).astype(jnp.bfloat16),
        all_orbitals,
        preferred_element_type=jnp.float32,
    )
    pick_pot = (
        multipole[:, None] == jnp.arange(potentials.shape[0], dtype=jnp.int32)[None, :]
    ).astype(jnp.float32)
    pot_rows = jnp.dot(pick_pot, potentials, precision=lax.Precision.HIGHEST)
    radial = coefs[:, 0:1] * pot_rows + coefs[:, 1:2] * (first_rows * second_rows)
    slot_weight = jnp.dot(
        matches.astype(jnp.float32), radial, precision=lax.Precision.HIGHEST
    ).astype(jnp.bfloat16)
    offset = jnp.mod(second_chan // col_devs - first_chan // col_devs, col_groups)
    block_index = first_chan // row_devs * BAND + offset
    slot_ids = jnp.max(jnp.where(matches, block_index[None, :], -1), axis=1)

    width = -(-(point_count + 1) // 128) * 128
    small = jnp.concatenate(
        [
            slot_weight,
            slot_ids.astype(jnp.bfloat16)[:, None],
            jnp.zeros((slot_count, width - point_count - 1), jnp.bfloat16),
        ],
        axis=1,
    )
    received_small = lax.all_to_all(small, ("prow", "pcol"), 0, 0, tiled=True)

    idents = received_small[:, point_count].astype(jnp.float32).astype(jnp.int32)
    select = (jnp.arange(block_count, dtype=jnp.int32)[:, None] == idents[None, :]).astype(
        jnp.bfloat16
    )
    weight_sum = jnp.dot(
        select, received_small[:, :point_count], preferred_element_type=jnp.float32
    )
    exchange_sum = jnp.einsum(
        "gs,sqb->qgb", select, received_exchange, preferred_element_type=jnp.float32
    )
    blocks = build_blocks(weight_sum, exchange_sum, basis)
    return blocks.reshape(RBLK, 1, BAND, 1, spline_count, spline_count)


def solution(mesh):
    placed = (
        P(),
        P(),
        P("pcol", None),
        P(),
        P(("prow", "pcol"), None),
        P(("prow", "pcol")),
        P(("prow", "pcol"), None),
        P(("prow", "pcol"), None, None),
    )
    return jax.shard_map(
        on_device,
        mesh=mesh,
        in_specs=placed,
        out_specs=P(None, "prow", None, "pcol", None, None),
        check_vma=False,
    )
```

```python
import jax
import jax.numpy as jnp
from jax import lax
from jax.experimental import pallas as pl
from jax.sharding import PartitionSpec as P

CAP = 2
BAND = 2
RBLK = 32


def split_bf16(values):
    high = values.astype(jnp.bfloat16)
    low = (values - high.astype(jnp.float32)).astype(jnp.bfloat16)
    return high, low


def tile_kernel(weight_ref, exchange_ref, basis_t_ref, basis_ref, inner_t_ref, out_ref):
    basis_t = basis_t_ref[...]
    basis = basis_ref[...]
    inner_t = inner_t_ref[...]
    for j in range(out_ref.shape[0]):
        left = (basis_t * weight_ref[j : j + 1, :]).astype(jnp.bfloat16)
        acc = jnp.dot(left, basis, preferred_element_type=jnp.float32)
        exchange_high, exchange_low = split_bf16(exchange_ref[:, j, :])
        acc += jnp.dot(inner_t, exchange_high, preferred_element_type=jnp.float32)
        acc += jnp.dot(inner_t, exchange_low, preferred_element_type=jnp.float32)
        out_ref[j] = acc.astype(out_ref.dtype)


def build_blocks(weight_sum, exchange_sum, basis, group=8):
    block_count, point_count = weight_sum.shape
    inner_count, _, spline_count = exchange_sum.shape
    basis_t = basis.T.astype(jnp.float32)
    inner_t = basis[:inner_count].T
    return pl.pallas_call(
        tile_kernel,
        grid=(block_count // group,),
        in_specs=[
            pl.BlockSpec((group, point_count), lambda g: (g, 0)),
            pl.BlockSpec((inner_count, group, spline_count), lambda g: (0, g, 0)),
            pl.BlockSpec((spline_count, point_count), lambda g: (0, 0)),
            pl.BlockSpec((point_count, spline_count), lambda g: (0, 0)),
            pl.BlockSpec((spline_count, inner_count), lambda g: (0, 0)),
        ],
        out_specs=pl.BlockSpec((group, spline_count, spline_count), lambda g: (g, 0, 0)),
        out_shape=jax.ShapeDtypeStruct((block_count, spline_count, spline_count), jnp.bfloat16),
    )(weight_sum, exchange_sum, basis_t, basis, inner_t)


def on_device(basis, potentials, orbitals, chan_orbital, pair_list, slot_list, coefs, exchange_ops):
    row_devs = lax.axis_size("prow")
    col_devs = lax.axis_size("pcol")
    slot_count = row_devs * col_devs * CAP
    chan_count = chan_orbital.shape[0]
    point_count = basis.shape[0]
    spline_count = basis.shape[1]
    inner_count = exchange_ops.shape[1]
    col_groups = chan_count // col_devs
    block_count = RBLK * BAND
    first_chan = pair_list[:, 0]
    second_chan = pair_list[:, 1]
    multipole = pair_list[:, 2]
    matches = slot_list[None, :] == jnp.arange(slot_count, dtype=jnp.int32)[:, None]

    slot_exchange = jnp.einsum(
        "st,tqb->sqb",
        matches.astype(jnp.bfloat16),
        exchange_ops,
        preferred_element_type=jnp.float32,
    ).astype(jnp.bfloat16)
    received_exchange = lax.all_to_all(slot_exchange, ("prow", "pcol"), 0, 0, tiled=True)

    channels = jnp.arange(chan_count, dtype=jnp.int32)
    first_orb = jnp.sum(
        jnp.where(first_chan[:, None] == channels[None, :], chan_orbital[None, :], 0), axis=1
    )
    second_orb = jnp.sum(
        jnp.where(second_chan[:, None] == channels[None, :], chan_orbital[None, :], 0), axis=1
    )
    match_float = matches.astype(jnp.float32)
    pick_pot = (
        multipole[:, None] == jnp.arange(potentials.shape[0], dtype=jnp.int32)[None, :]
    ).astype(jnp.float32)
    slot_pot_coef = jnp.dot(
        match_float * coefs[None, :, 0], pick_pot, precision=lax.Precision.HIGHEST
    )
    slot_pot = jnp.dot(slot_pot_coef, potentials, precision=lax.Precision.HIGHEST)
    slot_orb_coef = jnp.dot(match_float, coefs[:, 1], precision=lax.Precision.HIGHEST)
    offset = jnp.mod(second_chan // col_devs - first_chan // col_devs, col_groups)
    block_index = first_chan // row_devs * BAND + offset

    def per_slot(values):
        return jnp.max(jnp.where(matches, values[None, :], -1), axis=1).astype(jnp.float32)

    tail = jnp.stack(
        [slot_orb_coef, per_slot(first_orb), per_slot(second_orb), per_slot(block_index)], axis=1
    )
    width = -(-(point_count + tail.shape[1]) // 128) * 128
    small = jnp.concatenate(
        [
            slot_pot,
            tail,
            jnp.zeros((slot_count, width - point_count - tail.shape[1]), jnp.float32),
        ],
        axis=1,
    )
    received_small = lax.all_to_all(small, ("prow", "pcol"), 0, 0, tiled=True)

    all_orbitals = lax.all_gather(orbitals, "pcol", axis=0, tiled=True)
    orb_ids = jnp.arange(all_orbitals.shape[0], dtype=jnp.int32)
    recv_first = received_small[:, point_count + 1].astype(jnp.int32)
    recv_second = received_small[:, point_count + 2].astype(jnp.int32)
    idents = received_small[:, point_count + 3].astype(jnp.int32)
    first_rows = jnp.dot(
        (recv_first[:, None] == orb_ids[None, :]).astype(jnp.bfloat16),
        all_orbitals,
        preferred_element_type=jnp.float32,
    )
    second_rows = jnp.dot(
        (recv_second[:, None] == orb_ids[None, :]).astype(jnp.bfloat16),
        all_orbitals,
        preferred_element_type=jnp.float32,
    )
    slot_weight = (
        received_small[:, :point_count]
        + received_small[:, point_count : point_count + 1] * (first_rows * second_rows)
    ).astype(jnp.bfloat16)

    select = (jnp.arange(block_count, dtype=jnp.int32)[:, None] == idents[None, :]).astype(
        jnp.bfloat16
    )
    weight_sum = jnp.dot(select, slot_weight, preferred_element_type=jnp.float32)
    exchange_sum = jnp.einsum(
        "gs,sqb->qgb", select, received_exchange, preferred_element_type=jnp.float32
    )
    blocks = build_blocks(weight_sum, exchange_sum, basis)
    return blocks.reshape(RBLK, 1, BAND, 1, spline_count, spline_count)


def solution(mesh):
    placed = (
        P(),
        P(),
        P("pcol", None),
        P(),
        P(("prow", "pcol"), None),
        P(("prow", "pcol")),
        P(("prow", "pcol"), None),
        P(("prow", "pcol"), None, None),
    )
    return jax.shard_map(
        on_device,
        mesh=mesh,
        in_specs=placed,
        out_specs=P(None, "prow", None, "pcol", None, None),
        check_vma=False,
    )
```

```python
import jax
import jax.numpy as jnp
from jax import lax
from jax.experimental import pallas as pl
from jax.experimental.pallas import tpu as pltpu
from jax.sharding import PartitionSpec as P

CAP = 2
BAND = 2
RBLK = 32


def split_bf16(values):
    high = values.astype(jnp.bfloat16)
    low = (values - high.astype(jnp.float32)).astype(jnp.bfloat16)
    return high, low


def tile_kernel(weight_ref, exchange_ref, basis_t_ref, basis_ref, inner_t_ref, out_ref, lhs_ref, rhs_ref):
    point_count = basis_ref.shape[0]
    inner_count = inner_t_ref.shape[1]
    lhs_ref[:, point_count : point_count + inner_count] = inner_t_ref[...]
    lhs_ref[:, point_count + inner_count :] = inner_t_ref[...]
    rhs_ref[:point_count, :] = basis_ref[...]
    basis_t = basis_t_ref[...]
    for j in range(out_ref.shape[0]):
        lhs_ref[:, :point_count] = (basis_t * weight_ref[j : j + 1, :]).astype(jnp.bfloat16)
        exchange_high, exchange_low = split_bf16(exchange_ref[:, j, :])
        rhs_ref[point_count : point_count + inner_count, :] = exchange_high
        rhs_ref[point_count + inner_count :, :] = exchange_low
        acc = jnp.dot(lhs_ref[...], rhs_ref[...], preferred_element_type=jnp.float32)
        out_ref[j] = acc.astype(out_ref.dtype)


def build_blocks(weight_sum, exchange_sum, basis, group=8):
    block_count, point_count = weight_sum.shape
    inner_count, _, spline_count = exchange_sum.shape
    basis_t = basis.T.astype(jnp.float32)
    inner_t = basis[:inner_count].T
    depth = point_count + 2 * inner_count
    return pl.pallas_call(
        tile_kernel,
        grid=(block_count // group,),
        in_specs=[
            pl.BlockSpec((group, point_count), lambda g: (g, 0)),
            pl.BlockSpec((inner_count, group, spline_count), lambda g: (0, g, 0)),
            pl.BlockSpec((spline_count, point_count), lambda g: (0, 0)),
            pl.BlockSpec((point_count, spline_count), lambda g: (0, 0)),
            pl.BlockSpec((spline_count, inner_count), lambda g: (0, 0)),
        ],
        out_specs=pl.BlockSpec((group, spline_count, spline_count), lambda g: (g, 0, 0)),
        out_shape=jax.ShapeDtypeStruct((block_count, spline_count, spline_count), jnp.bfloat16),
        scratch_shapes=[
            pltpu.VMEM((spline_count, depth), jnp.bfloat16),
            pltpu.VMEM((depth, spline_count), jnp.bfloat16),
        ],
    )(weight_sum, exchange_sum, basis_t, basis, inner_t)


def on_device(basis, potentials, orbitals, chan_orbital, pair_list, slot_list, coefs, exchange_ops):
    row_devs = lax.axis_size("prow")
    col_devs = lax.axis_size("pcol")
    slot_count = row_devs * col_devs * CAP
    chan_count = chan_orbital.shape[0]
    point_count = basis.shape[0]
    spline_count = basis.shape[1]
    inner_count = exchange_ops.shape[1]
    col_groups = chan_count // col_devs
    block_count = RBLK * BAND
    first_chan = pair_list[:, 0]
    second_chan = pair_list[:, 1]
    multipole = pair_list[:, 2]
    matches = slot_list[None, :] == jnp.arange(slot_count, dtype=jnp.int32)[:, None]

    slot_exchange = jnp.einsum(
        "st,tqb->sqb",
        matches.astype(jnp.bfloat16),
        exchange_ops,
        preferred_element_type=jnp.float32,
    ).astype(jnp.bfloat16)
    received_exchange = lax.all_to_all(slot_exchange, ("prow", "pcol"), 0, 0, tiled=True)

    channels = jnp.arange(chan_count, dtype=jnp.int32)
    first_orb = jnp.sum(
        jnp.where(first_chan[:, None] == channels[None, :], chan_orbital[None, :], 0), axis=1
    )
    second_orb = jnp.sum(
        jnp.where(second_chan[:, None] == channels[None, :], chan_orbital[None, :], 0), axis=1
    )
    match_float = matches.astype(jnp.float32)
    pick_pot = (
        multipole[:, None] == jnp.arange(potentials.shape[0], dtype=jnp.int32)[None, :]
    ).astype(jnp.float32)
    slot_pot_coef = jnp.dot(
        match_float * coefs[None, :, 0], pick_pot, precision=lax.Precision.HIGHEST
    )
    slot_pot = jnp.dot(slot_pot_coef, potentials, precision=lax.Precision.HIGHEST)
    slot_orb_coef = jnp.dot(match_float, coefs[:, 1], precision=lax.Precision.HIGHEST)
    offset = jnp.mod(second_chan // col_devs - first_chan // col_devs, col_groups)
    block_index = first_chan // row_devs * BAND + offset

    def per_slot(values):
        return jnp.max(jnp.where(matches, values[None, :], -1), axis=1).astype(jnp.float32)

    tail = jnp.stack(
        [slot_orb_coef, per_slot(first_orb), per_slot(second_orb), per_slot(block_index)], axis=1
    )
    width = -(-(point_count + tail.shape[1]) // 128) * 128
    small = jnp.concatenate(
        [
            slot_pot,
            tail,
            jnp.zeros((slot_count, width - point_count - tail.shape[1]), jnp.float32),
        ],
        axis=1,
    )
    received_small = lax.all_to_all(small, ("prow", "pcol"), 0, 0, tiled=True)

    all_orbitals = lax.all_gather(orbitals, "pcol", axis=0, tiled=True)
    orb_ids = jnp.arange(all_orbitals.shape[0], dtype=jnp.int32)
    recv_first = received_small[:, point_count + 1].astype(jnp.int32)
    recv_second = received_small[:, point_count + 2].astype(jnp.int32)
    idents = received_small[:, point_count + 3].astype(jnp.int32)
    first_rows = jnp.dot(
        (recv_first[:, None] == orb_ids[None, :]).astype(jnp.bfloat16),
        all_orbitals,
        preferred_element_type=jnp.float32,
    )
    second_rows = jnp.dot(
        (recv_second[:, None] == orb_ids[None, :]).astype(jnp.bfloat16),
        all_orbitals,
        preferred_element_type=jnp.float32,
    )
    slot_weight = (
        received_small[:, :point_count]
        + received_small[:, point_count : point_count + 1] * (first_rows * second_rows)
    ).astype(jnp.bfloat16)

    select = (jnp.arange(block_count, dtype=jnp.int32)[:, None] == idents[None, :]).astype(
        jnp.bfloat16
    )
    weight_sum = jnp.dot(select, slot_weight, preferred_element_type=jnp.float32)
    exchange_sum = jnp.einsum(
        "gs,sqb->qgb", select, received_exchange, preferred_element_type=jnp.float32
    )
    blocks = build_blocks(weight_sum, exchange_sum, basis)
    return blocks.reshape(RBLK, 1, BAND, 1, spline_count, spline_count)


def solution(mesh):
    placed = (
        P(),
        P(),
        P("pcol", None),
        P(),
        P(("prow", "pcol"), None),
        P(("prow", "pcol")),
        P(("prow", "pcol"), None),
        P(("prow", "pcol"), None, None),
    )
    return jax.shard_map(
        on_device,
        mesh=mesh,
        in_specs=placed,
        out_specs=P(None, "prow", None, "pcol", None, None),
        check_vma=False,
    )
```

```python
import jax
import jax.numpy as jnp
from jax import lax
from jax.experimental import pallas as pl
from jax.experimental.pallas import tpu as pltpu
from jax.sharding import PartitionSpec as P

CAP = 2
BAND = 2
RBLK = 32


def split_bf16(values):
    high = values.astype(jnp.bfloat16)
    low = (values - high.astype(jnp.float32)).astype(jnp.bfloat16)
    return high, low


def local_kernel(weight_ref, basis_t_ref, basis_ref, out_ref):
    basis_t = basis_t_ref[...]
    basis = basis_ref[...]
    for j in range(out_ref.shape[0]):
        left = (basis_t * weight_ref[j : j + 1, :]).astype(jnp.bfloat16)
        out_ref[j] = jnp.dot(left, basis, preferred_element_type=jnp.float32)


def exchange_kernel(local_ref, exchange_ref, inner_t_ref, out_ref, lhs_ref, rhs_ref):
    inner_count = inner_t_ref.shape[1]
    lhs_ref[:, :inner_count] = inner_t_ref[...]
    lhs_ref[:, inner_count:] = inner_t_ref[...]
    for j in range(out_ref.shape[0]):
        exchange_high, exchange_low = split_bf16(exchange_ref[:, j, :])
        rhs_ref[:inner_count, :] = exchange_high
        rhs_ref[inner_count:, :] = exchange_low
        acc = local_ref[j] + jnp.dot(lhs_ref[...], rhs_ref[...], preferred_element_type=jnp.float32)
        out_ref[j] = acc.astype(out_ref.dtype)


def local_blocks(weight_sum, basis, group=8):
    block_count, point_count = weight_sum.shape
    spline_count = basis.shape[1]
    basis_t = basis.T.astype(jnp.float32)
    return pl.pallas_call(
        local_kernel,
        grid=(block_count // group,),
        in_specs=[
            pl.BlockSpec((group, point_count), lambda g: (g, 0)),
            pl.BlockSpec((spline_count, point_count), lambda g: (0, 0)),
            pl.BlockSpec((point_count, spline_count), lambda g: (0, 0)),
        ],
        out_specs=pl.BlockSpec((group, spline_count, spline_count), lambda g: (g, 0, 0)),
        out_shape=jax.ShapeDtypeStruct((block_count, spline_count, spline_count), jnp.float32),
    )(weight_sum, basis_t, basis)


def finish_blocks(local, exchange_sum, basis, group=8):
    block_count, spline_count, _ = local.shape
    inner_count = exchange_sum.shape[0]
    inner_t = basis[:inner_count].T
    return pl.pallas_call(
        exchange_kernel,
        grid=(block_count // group,),
        in_specs=[
            pl.BlockSpec((group, spline_count, spline_count), lambda g: (g, 0, 0)),
            pl.BlockSpec((inner_count, group, spline_count), lambda g: (0, g, 0)),
            pl.BlockSpec((spline_count, inner_count), lambda g: (0, 0)),
        ],
        out_specs=pl.BlockSpec((group, spline_count, spline_count), lambda g: (g, 0, 0)),
        out_shape=jax.ShapeDtypeStruct((block_count, spline_count, spline_count), jnp.bfloat16),
        scratch_shapes=[
            pltpu.VMEM((spline_count, 2 * inner_count), jnp.bfloat16),
            pltpu.VMEM((2 * inner_count, spline_count), jnp.bfloat16),
        ],
    )(local, exchange_sum, inner_t)


def on_device(basis, potentials, orbitals, chan_orbital, pair_list, slot_list, coefs, exchange_ops):
    row_devs = lax.axis_size("prow")
    col_devs = lax.axis_size("pcol")
    slot_count = row_devs * col_devs * CAP
    chan_count = chan_orbital.shape[0]
    point_count = basis.shape[0]
    spline_count = basis.shape[1]
    inner_count = exchange_ops.shape[1]
    col_groups = chan_count // col_devs
    block_count = RBLK * BAND
    first_chan = pair_list[:, 0]
    second_chan = pair_list[:, 1]
    multipole = pair_list[:, 2]
    matches = slot_list[None, :] == jnp.arange(slot_count, dtype=jnp.int32)[:, None]

    slot_exchange = jnp.einsum(
        "st,tqb->sqb",
        matches.astype(jnp.bfloat16),
        exchange_ops,
        preferred_element_type=jnp.float32,
    ).astype(jnp.bfloat16)
    received_exchange = lax.all_to_all(slot_exchange, ("prow", "pcol"), 0, 0, tiled=True)

    channels = jnp.arange(chan_count, dtype=jnp.int32)
    first_orb = jnp.sum(
        jnp.where(first_chan[:, None] == channels[None, :], chan_orbital[None, :], 0), axis=1
    )
    second_orb = jnp.sum(
        jnp.where(second_chan[:, None] == channels[None, :], chan_orbital[None, :], 0), axis=1
    )
    match_float = matches.astype(jnp.float32)
    pick_pot = (
        multipole[:, None] == jnp.arange(potentials.shape[0], dtype=jnp.int32)[None, :]
    ).astype(jnp.float32)
    slot_pot_coef = jnp.dot(
        match_float * coefs[None, :, 0], pick_pot, precision=lax.Precision.HIGHEST
    )
    slot_pot = jnp.dot(slot_pot_coef, potentials, precision=lax.Precision.HIGHEST)
    slot_orb_coef = jnp.dot(match_float, coefs[:, 1], precision=lax.Precision.HIGHEST)
    offset = jnp.mod(second_chan // col_devs - first_chan // col_devs, col_groups)
    block_index = first_chan // row_devs * BAND + offset

    def per_slot(values):
        return jnp.max(jnp.where(matches, values[None, :], -1), axis=1).astype(jnp.float32)

    tail = jnp.stack(
        [slot_orb_coef, per_slot(first_orb), per_slot(second_orb), per_slot(block_index)], axis=1
    )
    width = -(-(point_count + tail.shape[1]) // 128) * 128
    small = jnp.concatenate(
        [
            slot_pot,
            tail,
            jnp.zeros((slot_count, width - point_count - tail.shape[1]), jnp.float32),
        ],
        axis=1,
    )
    received_small = lax.all_to_all(small, ("prow", "pcol"), 0, 0, tiled=True)

    all_orbitals = lax.all_gather(orbitals, "pcol", axis=0, tiled=True)
    orb_ids = jnp.arange(all_orbitals.shape[0], dtype=jnp.int32)
    recv_first = received_small[:, point_count + 1].astype(jnp.int32)
    recv_second = received_small[:, point_count + 2].astype(jnp.int32)
    idents = received_small[:, point_count + 3].astype(jnp.int32)
    first_rows = jnp.dot(
        (recv_first[:, None] == orb_ids[None, :]).astype(jnp.bfloat16),
        all_orbitals,
        preferred_element_type=jnp.float32,
    )
    second_rows = jnp.dot(
        (recv_second[:, None] == orb_ids[None, :]).astype(jnp.bfloat16),
        all_orbitals,
        preferred_element_type=jnp.float32,
    )
    slot_weight = (
        received_small[:, :point_count]
        + received_small[:, point_count : point_count + 1] * (first_rows * second_rows)
    ).astype(jnp.bfloat16)

    select = (jnp.arange(block_count, dtype=jnp.int32)[:, None] == idents[None, :]).astype(
        jnp.bfloat16
    )
    weight_sum = jnp.dot(select, slot_weight, preferred_element_type=jnp.float32)
    local = local_blocks(weight_sum, basis)
    exchange_sum = jnp.einsum(
        "gs,sqb->qgb", select, received_exchange, preferred_element_type=jnp.float32
    )
    blocks = finish_blocks(local, exchange_sum, basis)
    return blocks.reshape(RBLK, 1, BAND, 1, spline_count, spline_count)


def solution(mesh):
    placed = (
        P(),
        P(),
        P("pcol", None),
        P(),
        P(("prow", "pcol"), None),
        P(("prow", "pcol")),
        P(("prow", "pcol"), None),
        P(("prow", "pcol"), None, None),
    )
    return jax.shard_map(
        on_device,
        mesh=mesh,
        in_specs=placed,
        out_specs=P(None, "prow", None, "pcol", None, None),
        check_vma=False,
    )
```

```python
import jax
import jax.numpy as jnp
from jax import lax
from jax.experimental import pallas as pl
from jax.experimental.pallas import tpu as pltpu
from jax.sharding import PartitionSpec as P

CAP = 2
BAND = 2
RBLK = 32


def split_bf16(values):
    high = values.astype(jnp.bfloat16)
    low = (values - high.astype(jnp.float32)).astype(jnp.bfloat16)
    return high, low


def tile_kernel(weight_ref, exchange_ref, basis_t_ref, basis_ref, inner_t_ref, out_ref, lhs_ref, rhs_ref):
    point_count = basis_ref.shape[0]
    inner_count = inner_t_ref.shape[1]
    lhs_ref[:, point_count : point_count + inner_count] = inner_t_ref[...]
    lhs_ref[:, point_count + inner_count :] = inner_t_ref[...]
    rhs_ref[:point_count, :] = basis_ref[...]
    basis_t = basis_t_ref[...]
    for j in range(out_ref.shape[0]):
        lhs_ref[:, :point_count] = (basis_t * weight_ref[j : j + 1, :]).astype(jnp.bfloat16)
        exchange_high, exchange_low = split_bf16(exchange_ref[j])
        rhs_ref[point_count : point_count + inner_count, :] = exchange_high
        rhs_ref[point_count + inner_count :, :] = exchange_low
        acc = jnp.dot(lhs_ref[...], rhs_ref[...], preferred_element_type=jnp.float32)
        out_ref[j] = acc.astype(out_ref.dtype)


def build_blocks(weight_sum, exchange_sum, basis, group=8):
    block_count, point_count = weight_sum.shape
    inner_count, spline_count = exchange_sum.shape[1:]
    basis_t = basis.T.astype(jnp.float32)
    inner_t = basis[:inner_count].T
    depth = point_count + 2 * inner_count
    return pl.pallas_call(
        tile_kernel,
        grid=(block_count // group,),
        in_specs=[
            pl.BlockSpec((group, point_count), lambda g: (g, 0)),
            pl.BlockSpec((group, inner_count, spline_count), lambda g: (g, 0, 0)),
            pl.BlockSpec((spline_count, point_count), lambda g: (0, 0)),
            pl.BlockSpec((point_count, spline_count), lambda g: (0, 0)),
            pl.BlockSpec((spline_count, inner_count), lambda g: (0, 0)),
        ],
        out_specs=pl.BlockSpec((group, spline_count, spline_count), lambda g: (g, 0, 0)),
        out_shape=jax.ShapeDtypeStruct((block_count, spline_count, spline_count), jnp.bfloat16),
        scratch_shapes=[
            pltpu.VMEM((spline_count, depth), jnp.bfloat16),
            pltpu.VMEM((depth, spline_count), jnp.bfloat16),
        ],
    )(weight_sum, exchange_sum, basis_t, basis, inner_t)


def on_device(basis, potentials, orbitals, chan_orbital, pair_list, slot_list, coefs, exchange_ops):
    row_devs = lax.axis_size("prow")
    col_devs = lax.axis_size("pcol")
    slot_count = row_devs * col_devs * CAP
    chan_count = chan_orbital.shape[0]
    point_count = basis.shape[0]
    spline_count = basis.shape[1]
    inner_count = exchange_ops.shape[1]
    col_groups = chan_count // col_devs
    block_count = RBLK * BAND
    first_chan = pair_list[:, 0]
    second_chan = pair_list[:, 1]
    multipole = pair_list[:, 2]
    matches = slot_list[None, :] == jnp.arange(slot_count, dtype=jnp.int32)[:, None]

    slot_exchange = jnp.einsum(
        "st,tqb->sqb",
        matches.astype(jnp.bfloat16),
        exchange_ops,
        preferred_element_type=jnp.float32,
    ).astype(jnp.bfloat16)
    received_exchange = lax.all_to_all(slot_exchange, ("prow", "pcol"), 0, 0, tiled=True)

    channels = jnp.arange(chan_count, dtype=jnp.int32)
    first_orb = jnp.sum(
        jnp.where(first_chan[:, None] == channels[None, :], chan_orbital[None, :], 0), axis=1
    )
    second_orb = jnp.sum(
        jnp.where(second_chan[:, None] == channels[None, :], chan_orbital[None, :], 0), axis=1
    )
    match_float = matches.astype(jnp.float32)
    pick_pot = (
        multipole[:, None] == jnp.arange(potentials.shape[0], dtype=jnp.int32)[None, :]
    ).astype(jnp.float32)
    slot_pot_coef = jnp.dot(
        match_float * coefs[None, :, 0], pick_pot, precision=lax.Precision.HIGHEST
    )
    slot_pot = jnp.dot(slot_pot_coef, potentials, precision=lax.Precision.HIGHEST)
    slot_orb_coef = jnp.dot(match_float, coefs[:, 1], precision=lax.Precision.HIGHEST)
    offset = jnp.mod(second_chan // col_devs - first_chan // col_devs, col_groups)
    block_index = first_chan // row_devs * BAND + offset

    def per_slot(values):
        return jnp.max(jnp.where(matches, values[None, :], -1), axis=1).astype(jnp.float32)

    tail = jnp.stack(
        [slot_orb_coef, per_slot(first_orb), per_slot(second_orb), per_slot(block_index)], axis=1
    )
    width = -(-(point_count + tail.shape[1]) // 128) * 128
    small = jnp.concatenate(
        [
            slot_pot,
            tail,
            jnp.zeros((slot_count, width - point_count - tail.shape[1]), jnp.float32),
        ],
        axis=1,
    )
    received_small = lax.all_to_all(small, ("prow", "pcol"), 0, 0, tiled=True)

    all_orbitals = lax.all_gather(orbitals, "pcol", axis=0, tiled=True)
    orb_ids = jnp.arange(all_orbitals.shape[0], dtype=jnp.int32)
    recv_first = received_small[:, point_count + 1].astype(jnp.int32)
    recv_second = received_small[:, point_count + 2].astype(jnp.int32)
    idents = received_small[:, point_count + 3].astype(jnp.int32)
    first_rows = jnp.dot(
        (recv_first[:, None] == orb_ids[None, :]).astype(jnp.bfloat16),
        all_orbitals,
        preferred_element_type=jnp.float32,
    )
    second_rows = jnp.dot(
        (recv_second[:, None] == orb_ids[None, :]).astype(jnp.bfloat16),
        all_orbitals,
        preferred_element_type=jnp.float32,
    )
    slot_weight = (
        received_small[:, :point_count]
        + received_small[:, point_count : point_count + 1] * (first_rows * second_rows)
    ).astype(jnp.bfloat16)

    select = (jnp.arange(block_count, dtype=jnp.int32)[:, None] == idents[None, :]).astype(
        jnp.bfloat16
    )
    weight_sum = jnp.dot(select, slot_weight, preferred_element_type=jnp.float32)
    exchange_sum = jnp.einsum(
        "gs,sqb->gqb", select, received_exchange, preferred_element_type=jnp.float32
    )
    blocks = build_blocks(weight_sum, exchange_sum, basis)
    return blocks.reshape(RBLK, 1, BAND, 1, spline_count, spline_count)


def solution(mesh):
    placed = (
        P(),
        P(),
        P("pcol", None),
        P(),
        P(("prow", "pcol"), None),
        P(("prow", "pcol")),
        P(("prow", "pcol"), None),
        P(("prow", "pcol"), None, None),
    )
    return jax.shard_map(
        on_device,
        mesh=mesh,
        in_specs=placed,
        out_specs=P(None, "prow", None, "pcol", None, None),
        check_vma=False,
    )
```

```python
import jax
import jax.numpy as jnp
from jax import lax
from jax.experimental import pallas as pl
from jax.experimental.pallas import tpu as pltpu
from jax.sharding import PartitionSpec as P

CAP = 2
BAND = 2
RBLK = 32


def split_bf16(values):
    high = values.astype(jnp.bfloat16)
    low = (values - high.astype(jnp.float32)).astype(jnp.bfloat16)
    return high, low


def tile_kernel(weight_ref, exchange_ref, basis_t_ref, basis_ref, inner_t_ref, out_ref, lhs_ref, rhs_ref):
    point_count = basis_ref.shape[0]
    inner_count = inner_t_ref.shape[1]
    lhs_ref[:, point_count : point_count + inner_count] = inner_t_ref[...]
    lhs_ref[:, point_count + inner_count :] = inner_t_ref[...]
    rhs_ref[:point_count, :] = basis_ref[...]
    basis_t = basis_t_ref[...]
    for j in range(out_ref.shape[0]):
        lhs_ref[:, :point_count] = (basis_t * weight_ref[j : j + 1, :]).astype(jnp.bfloat16)
        exchange_high, exchange_low = split_bf16(exchange_ref[j])
        rhs_ref[point_count : point_count + inner_count, :] = exchange_high
        rhs_ref[point_count + inner_count :, :] = exchange_low
        acc = jnp.dot(lhs_ref[...], rhs_ref[...], preferred_element_type=jnp.float32)
        out_ref[j] = acc.astype(out_ref.dtype)


def build_blocks(weight_sum, exchange_sum, basis, group=8):
    block_count, point_count = weight_sum.shape
    inner_count, spline_count = exchange_sum.shape[1:]
    basis_t = basis.T.astype(jnp.float32)
    inner_t = basis[:inner_count].T
    depth = point_count + 2 * inner_count
    return pl.pallas_call(
        tile_kernel,
        grid=(block_count // group,),
        in_specs=[
            pl.BlockSpec((group, point_count), lambda g: (g, 0)),
            pl.BlockSpec((group, inner_count, spline_count), lambda g: (g, 0, 0)),
            pl.BlockSpec((spline_count, point_count), lambda g: (0, 0)),
            pl.BlockSpec((point_count, spline_count), lambda g: (0, 0)),
            pl.BlockSpec((spline_count, inner_count), lambda g: (0, 0)),
        ],
        out_specs=pl.BlockSpec((group, spline_count, spline_count), lambda g: (g, 0, 0)),
        out_shape=jax.ShapeDtypeStruct((block_count, spline_count, spline_count), jnp.bfloat16),
        scratch_shapes=[
            pltpu.VMEM((spline_count, depth), jnp.bfloat16),
            pltpu.VMEM((depth, spline_count), jnp.bfloat16),
        ],
    )(weight_sum, exchange_sum, basis_t, basis, inner_t)


def on_device(basis, potentials, orbitals, chan_orbital, pair_list, slot_list, coefs, exchange_ops):
    row_devs = lax.axis_size("prow")
    col_devs = lax.axis_size("pcol")
    slot_count = row_devs * col_devs * CAP
    chan_count = chan_orbital.shape[0]
    point_count = basis.shape[0]
    spline_count = basis.shape[1]
    inner_count = exchange_ops.shape[1]
    col_groups = chan_count // col_devs
    block_count = RBLK * BAND
    first_chan = pair_list[:, 0]
    second_chan = pair_list[:, 1]
    multipole = pair_list[:, 2]
    matches = slot_list[None, :] == jnp.arange(slot_count, dtype=jnp.int32)[:, None]

    slot_exchange = jnp.einsum(
        "st,tqb->sqb",
        matches.astype(jnp.bfloat16),
        exchange_ops,
        preferred_element_type=jnp.float32,
    ).astype(jnp.bfloat16)
    orb_local = orbitals.shape[0]
    all_orbitals = lax.dynamic_update_slice_in_dim(
        jnp.zeros((orb_local * col_devs, orbitals.shape[1]), orbitals.dtype),
        orbitals,
        lax.axis_index("pcol") * orb_local,
        0,
    )
    shift = 1
    while shift < col_devs:
        pairs = [(i, (i + shift) % col_devs) for i in range(col_devs)]
        all_orbitals = all_orbitals + lax.ppermute(all_orbitals, "pcol", pairs)
        shift *= 2
    slot_exchange, all_orbitals = lax.optimization_barrier((slot_exchange, all_orbitals))
    received_exchange = lax.all_to_all(slot_exchange, ("prow", "pcol"), 0, 0, tiled=True)

    channels = jnp.arange(chan_count, dtype=jnp.int32)
    first_orb = jnp.sum(
        jnp.where(first_chan[:, None] == channels[None, :], chan_orbital[None, :], 0), axis=1
    )
    second_orb = jnp.sum(
        jnp.where(second_chan[:, None] == channels[None, :], chan_orbital[None, :], 0), axis=1
    )
    match_float = matches.astype(jnp.float32)
    pick_pot = (
        multipole[:, None] == jnp.arange(potentials.shape[0], dtype=jnp.int32)[None, :]
    ).astype(jnp.float32)
    slot_pot_coef = jnp.dot(
        match_float * coefs[None, :, 0], pick_pot, precision=lax.Precision.HIGHEST
    )
    slot_pot = jnp.dot(slot_pot_coef, potentials, precision=lax.Precision.HIGHEST)
    slot_orb_coef = jnp.dot(match_float, coefs[:, 1], precision=lax.Precision.HIGHEST)
    offset = jnp.mod(second_chan // col_devs - first_chan // col_devs, col_groups)
    block_index = first_chan // row_devs * BAND + offset

    def per_slot(values):
        return jnp.max(jnp.where(matches, values[None, :], -1), axis=1).astype(jnp.float32)

    tail = jnp.stack(
        [slot_orb_coef, per_slot(first_orb), per_slot(second_orb), per_slot(block_index)], axis=1
    )
    width = -(-(point_count + tail.shape[1]) // 128) * 128
    small = jnp.concatenate(
        [
            slot_pot,
            tail,
            jnp.zeros((slot_count, width - point_count - tail.shape[1]), jnp.float32),
        ],
        axis=1,
    )
    received_small = lax.all_to_all(small, ("prow", "pcol"), 0, 0, tiled=True)

    orb_ids = jnp.arange(all_orbitals.shape[0], dtype=jnp.int32)
    recv_first = received_small[:, point_count + 1].astype(jnp.int32)
    recv_second = received_small[:, point_count + 2].astype(jnp.int32)
    idents = received_small[:, point_count + 3].astype(jnp.int32)
    first_rows = jnp.dot(
        (recv_first[:, None] == orb_ids[None, :]).astype(jnp.bfloat16),
        all_orbitals,
        preferred_element_type=jnp.float32,
    )
    second_rows = jnp.dot(
        (recv_second[:, None] == orb_ids[None, :]).astype(jnp.bfloat16),
        all_orbitals,
        preferred_element_type=jnp.float32,
    )
    slot_weight = (
        received_small[:, :point_count]
        + received_small[:, point_count : point_count + 1] * (first_rows * second_rows)
    ).astype(jnp.bfloat16)

    select = (jnp.arange(block_count, dtype=jnp.int32)[:, None] == idents[None, :]).astype(
        jnp.bfloat16
    )
    weight_sum = jnp.dot(select, slot_weight, preferred_element_type=jnp.float32)
    exchange_sum = jnp.einsum(
        "gs,sqb->gqb", select, received_exchange, preferred_element_type=jnp.float32
    )
    blocks = build_blocks(weight_sum, exchange_sum, basis)
    return blocks.reshape(RBLK, 1, BAND, 1, spline_count, spline_count)


def solution(mesh):
    placed = (
        P(),
        P(),
        P("pcol", None),
        P(),
        P(("prow", "pcol"), None),
        P(("prow", "pcol")),
        P(("prow", "pcol"), None),
        P(("prow", "pcol"), None, None),
    )
    return jax.shard_map(
        on_device,
        mesh=mesh,
        in_specs=placed,
        out_specs=P(None, "prow", None, "pcol", None, None),
        check_vma=False,
    )
```

```python
import jax
import jax.numpy as jnp
from jax import lax
from jax.experimental import pallas as pl
from jax.experimental.pallas import tpu as pltpu
from jax.sharding import PartitionSpec as P

CAP = 2
BAND = 2
RBLK = 32


def split_bf16(values):
    high = values.astype(jnp.bfloat16)
    low = (values - high.astype(jnp.float32)).astype(jnp.bfloat16)
    return high, low


def tile_kernel(weight_ref, exchange_ref, basis_t_ref, basis_ref, inner_t_ref, out_ref, lhs_ref, rhs_ref):
    point_count = basis_ref.shape[0]
    inner_count = inner_t_ref.shape[1]
    lhs_ref[:, point_count : point_count + inner_count] = inner_t_ref[...]
    lhs_ref[:, point_count + inner_count :] = inner_t_ref[...]
    rhs_ref[:point_count, :] = basis_ref[...]
    basis_t = basis_t_ref[...]
    for j in range(out_ref.shape[0]):
        lhs_ref[:, :point_count] = (basis_t * weight_ref[j : j + 1, :]).astype(jnp.bfloat16)
        exchange_high, exchange_low = split_bf16(exchange_ref[j])
        rhs_ref[point_count : point_count + inner_count, :] = exchange_high
        rhs_ref[point_count + inner_count :, :] = exchange_low
        acc = jnp.dot(lhs_ref[...], rhs_ref[...], preferred_element_type=jnp.float32)
        out_ref[j] = acc.astype(out_ref.dtype)


def build_blocks(weight_sum, exchange_sum, basis, group=8):
    block_count, point_count = weight_sum.shape
    inner_count, spline_count = exchange_sum.shape[1:]
    basis_t = basis.T.astype(jnp.float32)
    inner_t = basis[:inner_count].T
    depth = point_count + 2 * inner_count
    return pl.pallas_call(
        tile_kernel,
        grid=(block_count // group,),
        in_specs=[
            pl.BlockSpec((group, point_count), lambda g: (g, 0)),
            pl.BlockSpec((group, inner_count, spline_count), lambda g: (g, 0, 0)),
            pl.BlockSpec((spline_count, point_count), lambda g: (0, 0)),
            pl.BlockSpec((point_count, spline_count), lambda g: (0, 0)),
            pl.BlockSpec((spline_count, inner_count), lambda g: (0, 0)),
        ],
        out_specs=pl.BlockSpec((group, spline_count, spline_count), lambda g: (g, 0, 0)),
        out_shape=jax.ShapeDtypeStruct((block_count, spline_count, spline_count), jnp.bfloat16),
        scratch_shapes=[
            pltpu.VMEM((spline_count, depth), jnp.bfloat16),
            pltpu.VMEM((depth, spline_count), jnp.bfloat16),
        ],
    )(weight_sum, exchange_sum, basis_t, basis, inner_t)


def on_device(basis, potentials, orbitals, chan_orbital, pair_list, slot_list, coefs, exchange_ops):
    row_devs = lax.axis_size("prow")
    col_devs = lax.axis_size("pcol")
    slot_count = row_devs * col_devs * CAP
    chan_count = chan_orbital.shape[0]
    point_count = basis.shape[0]
    spline_count = basis.shape[1]
    inner_count = exchange_ops.shape[1]
    col_groups = chan_count // col_devs
    block_count = RBLK * BAND
    first_chan = pair_list[:, 0]
    second_chan = pair_list[:, 1]
    multipole = pair_list[:, 2]
    matches = slot_list[None, :] == jnp.arange(slot_count, dtype=jnp.int32)[:, None]

    slot_exchange = jnp.einsum(
        "st,tqb->sqb",
        matches.astype(jnp.bfloat16),
        exchange_ops,
        preferred_element_type=jnp.float32,
    ).astype(jnp.bfloat16)
    orb_local = orbitals.shape[0]
    col_index = lax.axis_index("pcol")
    all_orbitals = lax.dynamic_update_slice_in_dim(
        jnp.zeros((orb_local * col_devs, orbitals.shape[1]), orbitals.dtype),
        orbitals,
        col_index * orb_local,
        0,
    )
    for shift in range(1, col_devs):
        pairs = [(i, (i + shift) % col_devs) for i in range(col_devs)]
        all_orbitals = lax.dynamic_update_slice_in_dim(
            all_orbitals,
            lax.ppermute(orbitals, "pcol", pairs),
            ((col_index - shift) % col_devs) * orb_local,
            0,
        )
    slot_exchange, all_orbitals = lax.optimization_barrier((slot_exchange, all_orbitals))
    received_exchange = lax.all_to_all(slot_exchange, ("prow", "pcol"), 0, 0, tiled=True)

    channels = jnp.arange(chan_count, dtype=jnp.int32)
    first_orb = jnp.sum(
        jnp.where(first_chan[:, None] == channels[None, :], chan_orbital[None, :], 0), axis=1
    )
    second_orb = jnp.sum(
        jnp.where(second_chan[:, None] == channels[None, :], chan_orbital[None, :], 0), axis=1
    )
    match_float = matches.astype(jnp.float32)
    pick_pot = (
        multipole[:, None] == jnp.arange(potentials.shape[0], dtype=jnp.int32)[None, :]
    ).astype(jnp.float32)
    slot_pot_coef = jnp.dot(
        match_float * coefs[None, :, 0], pick_pot, precision=lax.Precision.HIGHEST
    )
    slot_pot = jnp.dot(slot_pot_coef, potentials, precision=lax.Precision.HIGHEST)
    slot_orb_coef = jnp.dot(match_float, coefs[:, 1], precision=lax.Precision.HIGHEST)
    offset = jnp.mod(second_chan // col_devs - first_chan // col_devs, col_groups)
    block_index = first_chan // row_devs * BAND + offset

    def per_slot(values):
        return jnp.max(jnp.where(matches, values[None, :], -1), axis=1).astype(jnp.float32)

    tail = jnp.stack(
        [slot_orb_coef, per_slot(first_orb), per_slot(second_orb), per_slot(block_index)], axis=1
    )
    width = -(-(point_count + tail.shape[1]) // 128) * 128
    small = jnp.concatenate(
        [
            slot_pot,
            tail,
            jnp.zeros((slot_count, width - point_count - tail.shape[1]), jnp.float32),
        ],
        axis=1,
    )
    received_small = lax.all_to_all(small, ("prow", "pcol"), 0, 0, tiled=True)

    orb_ids = jnp.arange(all_orbitals.shape[0], dtype=jnp.int32)
    recv_first = received_small[:, point_count + 1].astype(jnp.int32)
    recv_second = received_small[:, point_count + 2].astype(jnp.int32)
    idents = received_small[:, point_count + 3].astype(jnp.int32)
    first_rows = jnp.dot(
        (recv_first[:, None] == orb_ids[None, :]).astype(jnp.bfloat16),
        all_orbitals,
        preferred_element_type=jnp.float32,
    )
    second_rows = jnp.dot(
        (recv_second[:, None] == orb_ids[None, :]).astype(jnp.bfloat16),
        all_orbitals,
        preferred_element_type=jnp.float32,
    )
    slot_weight = (
        received_small[:, :point_count]
        + received_small[:, point_count : point_count + 1] * (first_rows * second_rows)
    ).astype(jnp.bfloat16)

    select = (jnp.arange(block_count, dtype=jnp.int32)[:, None] == idents[None, :]).astype(
        jnp.bfloat16
    )
    weight_sum = jnp.dot(select, slot_weight, preferred_element_type=jnp.float32)
    exchange_sum = jnp.einsum(
        "gs,sqb->gqb", select, received_exchange, preferred_element_type=jnp.float32
    )
    blocks = build_blocks(weight_sum, exchange_sum, basis)
    return blocks.reshape(RBLK, 1, BAND, 1, spline_count, spline_count)


def solution(mesh):
    placed = (
        P(),
        P(),
        P("pcol", None),
        P(),
        P(("prow", "pcol"), None),
        P(("prow", "pcol")),
        P(("prow", "pcol"), None),
        P(("prow", "pcol"), None, None),
    )
    return jax.shard_map(
        on_device,
        mesh=mesh,
        in_specs=placed,
        out_specs=P(None, "prow", None, "pcol", None, None),
        check_vma=False,
    )
```

```python
import jax
import jax.numpy as jnp
from jax import lax
from jax.experimental import pallas as pl
from jax.experimental.pallas import tpu as pltpu
from jax.sharding import PartitionSpec as P

CAP = 2
BAND = 2
RBLK = 32


def split_bf16(values):
    high = values.astype(jnp.bfloat16)
    low = (values - high.astype(jnp.float32)).astype(jnp.bfloat16)
    return high, low


def tile_kernel(weight_ref, exchange_ref, basis_t_ref, basis_ref, inner_t_ref, out_ref, lhs_ref, rhs_ref):
    point_count = basis_ref.shape[0]
    lhs_ref[:, point_count:] = inner_t_ref[...]
    rhs_ref[:point_count, :] = basis_ref[...]
    basis_t = basis_t_ref[...]
    for j in range(out_ref.shape[0]):
        lhs_ref[:, :point_count] = (basis_t * weight_ref[j : j + 1, :]).astype(jnp.bfloat16)
        rhs_ref[point_count:, :] = exchange_ref[j]
        acc = jnp.dot(lhs_ref[...], rhs_ref[...], preferred_element_type=jnp.float32)
        out_ref[j] = acc.astype(out_ref.dtype)


def build_blocks(weight_sum, exchange_sum, basis, group=8):
    block_count, point_count = weight_sum.shape
    inner_count, spline_count = exchange_sum.shape[1:]
    basis_t = basis.T.astype(jnp.float32)
    inner_t = basis[:inner_count].T
    depth = point_count + inner_count
    return pl.pallas_call(
        tile_kernel,
        grid=(block_count // group,),
        in_specs=[
            pl.BlockSpec((group, point_count), lambda g: (g, 0)),
            pl.BlockSpec((group, inner_count, spline_count), lambda g: (g, 0, 0)),
            pl.BlockSpec((spline_count, point_count), lambda g: (0, 0)),
            pl.BlockSpec((point_count, spline_count), lambda g: (0, 0)),
            pl.BlockSpec((spline_count, inner_count), lambda g: (0, 0)),
        ],
        out_specs=pl.BlockSpec((group, spline_count, spline_count), lambda g: (g, 0, 0)),
        out_shape=jax.ShapeDtypeStruct((block_count, spline_count, spline_count), jnp.bfloat16),
        scratch_shapes=[
            pltpu.VMEM((spline_count, depth), jnp.bfloat16),
            pltpu.VMEM((depth, spline_count), jnp.bfloat16),
        ],
    )(weight_sum, exchange_sum, basis_t, basis, inner_t)


def on_device(basis, potentials, orbitals, chan_orbital, pair_list, slot_list, coefs, exchange_ops):
    row_devs = lax.axis_size("prow")
    col_devs = lax.axis_size("pcol")
    slot_count = row_devs * col_devs * CAP
    chan_count = chan_orbital.shape[0]
    point_count = basis.shape[0]
    spline_count = basis.shape[1]
    inner_count = exchange_ops.shape[1]
    col_groups = chan_count // col_devs
    block_count = RBLK * BAND
    first_chan = pair_list[:, 0]
    second_chan = pair_list[:, 1]
    multipole = pair_list[:, 2]
    matches = slot_list[None, :] == jnp.arange(slot_count, dtype=jnp.int32)[:, None]

    slot_exchange = jnp.einsum(
        "st,tqb->sqb",
        matches.astype(jnp.bfloat16),
        exchange_ops,
        preferred_element_type=jnp.float32,
    ).astype(jnp.bfloat16)
    received_exchange = lax.all_to_all(slot_exchange, ("prow", "pcol"), 0, 0, tiled=True)

    channels = jnp.arange(chan_count, dtype=jnp.int32)
    first_orb = jnp.sum(
        jnp.where(first_chan[:, None] == channels[None, :], chan_orbital[None, :], 0), axis=1
    )
    second_orb = jnp.sum(
        jnp.where(second_chan[:, None] == channels[None, :], chan_orbital[None, :], 0), axis=1
    )
    match_float = matches.astype(jnp.float32)
    pick_pot = (
        multipole[:, None] == jnp.arange(potentials.shape[0], dtype=jnp.int32)[None, :]
    ).astype(jnp.float32)
    slot_pot_coef = jnp.dot(
        match_float * coefs[None, :, 0], pick_pot, precision=lax.Precision.HIGHEST
    )
    slot_pot = jnp.dot(slot_pot_coef, potentials, precision=lax.Precision.HIGHEST)
    slot_orb_coef = jnp.dot(match_float, coefs[:, 1], precision=lax.Precision.HIGHEST)
    offset = jnp.mod(second_chan // col_devs - first_chan // col_devs, col_groups)
    block_index = first_chan // row_devs * BAND + offset

    def per_slot(values):
        return jnp.max(jnp.where(matches, values[None, :], -1), axis=1).astype(jnp.float32)

    tail = jnp.stack(
        [slot_orb_coef, per_slot(first_orb), per_slot(second_orb), per_slot(block_index)], axis=1
    )
    width = -(-(point_count + tail.shape[1]) // 128) * 128
    small = jnp.concatenate(
        [
            slot_pot,
            tail,
            jnp.zeros((slot_count, width - point_count - tail.shape[1]), jnp.float32),
        ],
        axis=1,
    )
    received_small = lax.all_to_all(small, ("prow", "pcol"), 0, 0, tiled=True)

    all_orbitals = lax.all_gather(orbitals, "pcol", axis=0, tiled=True)
    orb_ids = jnp.arange(all_orbitals.shape[0], dtype=jnp.int32)
    recv_first = received_small[:, point_count + 1].astype(jnp.int32)
    recv_second = received_small[:, point_count + 2].astype(jnp.int32)
    idents = received_small[:, point_count + 3].astype(jnp.int32)
    first_rows = jnp.dot(
        (recv_first[:, None] == orb_ids[None, :]).astype(jnp.bfloat16),
        all_orbitals,
        preferred_element_type=jnp.float32,
    )
    second_rows = jnp.dot(
        (recv_second[:, None] == orb_ids[None, :]).astype(jnp.bfloat16),
        all_orbitals,
        preferred_element_type=jnp.float32,
    )
    slot_weight = (
        received_small[:, :point_count]
        + received_small[:, point_count : point_count + 1] * (first_rows * second_rows)
    ).astype(jnp.bfloat16)

    select = (jnp.arange(block_count, dtype=jnp.int32)[:, None] == idents[None, :]).astype(
        jnp.bfloat16
    )
    weight_sum = jnp.dot(select, slot_weight, preferred_element_type=jnp.float32)
    exchange_sum = jnp.einsum(
        "gs,sqb->gqb", select, received_exchange, preferred_element_type=jnp.float32
    ).astype(jnp.bfloat16)
    blocks = build_blocks(weight_sum, exchange_sum, basis)
    return blocks.reshape(RBLK, 1, BAND, 1, spline_count, spline_count)


def solution(mesh):
    placed = (
        P(),
        P(),
        P("pcol", None),
        P(),
        P(("prow", "pcol"), None),
        P(("prow", "pcol")),
        P(("prow", "pcol"), None),
        P(("prow", "pcol"), None, None),
    )
    return jax.shard_map(
        on_device,
        mesh=mesh,
        in_specs=placed,
        out_specs=P(None, "prow", None, "pcol", None, None),
        check_vma=False,
    )
```

```python
import jax
import jax.numpy as jnp
from jax import lax
from jax.experimental import pallas as pl
from jax.experimental.pallas import tpu as pltpu
from jax.sharding import PartitionSpec as P

CAP = 2
BAND = 2
RBLK = 32


def split_bf16(values):
    high = values.astype(jnp.bfloat16)
    low = (values - high.astype(jnp.float32)).astype(jnp.bfloat16)
    return high, low


def tile_kernel(weight_ref, exchange_ref, basis_t_ref, basis_ref, inner_t_ref, out_ref, lhs_ref, rhs_ref):
    point_count = basis_ref.shape[0]
    lhs_ref[:, point_count:] = inner_t_ref[...]
    rhs_ref[:point_count, :] = basis_ref[...]
    basis_t = basis_t_ref[...]
    for j in range(out_ref.shape[0]):
        lhs_ref[:, :point_count] = (basis_t * weight_ref[j : j + 1, :]).astype(jnp.bfloat16)
        rhs_ref[point_count:, :] = exchange_ref[j]
        acc = jnp.dot(lhs_ref[...], rhs_ref[...], preferred_element_type=jnp.float32)
        out_ref[j] = acc.astype(out_ref.dtype)


def build_blocks(weight_sum, exchange_sum, basis, group=16):
    block_count, point_count = weight_sum.shape
    inner_count, spline_count = exchange_sum.shape[1:]
    basis_t = basis.T.astype(jnp.float32)
    inner_t = basis[:inner_count].T
    depth = point_count + inner_count
    return pl.pallas_call(
        tile_kernel,
        grid=(block_count // group,),
        in_specs=[
            pl.BlockSpec((group, point_count), lambda g: (g, 0)),
            pl.BlockSpec((group, inner_count, spline_count), lambda g: (g, 0, 0)),
            pl.BlockSpec((spline_count, point_count), lambda g: (0, 0)),
            pl.BlockSpec((point_count, spline_count), lambda g: (0, 0)),
            pl.BlockSpec((spline_count, inner_count), lambda g: (0, 0)),
        ],
        out_specs=pl.BlockSpec((group, spline_count, spline_count), lambda g: (g, 0, 0)),
        out_shape=jax.ShapeDtypeStruct((block_count, spline_count, spline_count), jnp.bfloat16),
        scratch_shapes=[
            pltpu.VMEM((spline_count, depth), jnp.bfloat16),
            pltpu.VMEM((depth, spline_count), jnp.bfloat16),
        ],
    )(weight_sum, exchange_sum, basis_t, basis, inner_t)


def on_device(basis, potentials, orbitals, chan_orbital, pair_list, slot_list, coefs, exchange_ops):
    row_devs = lax.axis_size("prow")
    col_devs = lax.axis_size("pcol")
    slot_count = row_devs * col_devs * CAP
    chan_count = chan_orbital.shape[0]
    point_count = basis.shape[0]
    spline_count = basis.shape[1]
    inner_count = exchange_ops.shape[1]
    col_groups = chan_count // col_devs
    block_count = RBLK * BAND
    first_chan = pair_list[:, 0]
    second_chan = pair_list[:, 1]
    multipole = pair_list[:, 2]
    matches = slot_list[None, :] == jnp.arange(slot_count, dtype=jnp.int32)[:, None]

    slot_exchange = jnp.einsum(
        "st,tqb->sqb",
        matches.astype(jnp.bfloat16),
        exchange_ops,
        preferred_element_type=jnp.float32,
    ).astype(jnp.bfloat16)
    received_exchange = lax.all_to_all(slot_exchange, ("prow", "pcol"), 0, 0, tiled=True)

    channels = jnp.arange(chan_count, dtype=jnp.int32)
    first_orb = jnp.sum(
        jnp.where(first_chan[:, None] == channels[None, :], chan_orbital[None, :], 0), axis=1
    )
    second_orb = jnp.sum(
        jnp.where(second_chan[:, None] == channels[None, :], chan_orbital[None, :], 0), axis=1
    )
    match_float = matches.astype(jnp.float32)
    pick_pot = (
        multipole[:, None] == jnp.arange(potentials.shape[0], dtype=jnp.int32)[None, :]
    ).astype(jnp.float32)
    slot_pot_coef = jnp.dot(
        match_float * coefs[None, :, 0], pick_pot, precision=lax.Precision.HIGHEST
    )
    slot_pot = jnp.dot(slot_pot_coef, potentials, precision=lax.Precision.HIGHEST)
    slot_orb_coef = jnp.dot(match_float, coefs[:, 1], precision=lax.Precision.HIGHEST)
    offset = jnp.mod(second_chan // col_devs - first_chan // col_devs, col_groups)
    block_index = first_chan // row_devs * BAND + offset

    def per_slot(values):
        return jnp.max(jnp.where(matches, values[None, :], -1), axis=1).astype(jnp.float32)

    tail = jnp.stack(
        [slot_orb_coef, per_slot(first_orb), per_slot(second_orb), per_slot(block_index)], axis=1
    )
    width = -(-(point_count + tail.shape[1]) // 128) * 128
    small = jnp.concatenate(
        [
            slot_pot,
            tail,
            jnp.zeros((slot_count, width - point_count - tail.shape[1]), jnp.float32),
        ],
        axis=1,
    )
    received_small = lax.all_to_all(small, ("prow", "pcol"), 0, 0, tiled=True)

    all_orbitals = lax.all_gather(orbitals, "pcol", axis=0, tiled=True)
    orb_ids = jnp.arange(all_orbitals.shape[0], dtype=jnp.int32)
    recv_first = received_small[:, point_count + 1].astype(jnp.int32)
    recv_second = received_small[:, point_count + 2].astype(jnp.int32)
    idents = received_small[:, point_count + 3].astype(jnp.int32)
    first_rows = jnp.dot(
        (recv_first[:, None] == orb_ids[None, :]).astype(jnp.bfloat16),
        all_orbitals,
        preferred_element_type=jnp.float32,
    )
    second_rows = jnp.dot(
        (recv_second[:, None] == orb_ids[None, :]).astype(jnp.bfloat16),
        all_orbitals,
        preferred_element_type=jnp.float32,
    )
    slot_weight = (
        received_small[:, :point_count]
        + received_small[:, point_count : point_count + 1] * (first_rows * second_rows)
    ).astype(jnp.bfloat16)

    select = (jnp.arange(block_count, dtype=jnp.int32)[:, None] == idents[None, :]).astype(
        jnp.bfloat16
    )
    weight_sum = jnp.dot(select, slot_weight, preferred_element_type=jnp.float32)
    exchange_sum = jnp.einsum(
        "gs,sqb->gqb", select, received_exchange, preferred_element_type=jnp.float32
    ).astype(jnp.bfloat16)
    blocks = build_blocks(weight_sum, exchange_sum, basis)
    return blocks.reshape(RBLK, 1, BAND, 1, spline_count, spline_count)


def solution(mesh):
    placed = (
        P(),
        P(),
        P("pcol", None),
        P(),
        P(("prow", "pcol"), None),
        P(("prow", "pcol")),
        P(("prow", "pcol"), None),
        P(("prow", "pcol"), None, None),
    )
    return jax.shard_map(
        on_device,
        mesh=mesh,
        in_specs=placed,
        out_specs=P(None, "prow", None, "pcol", None, None),
        check_vma=False,
    )
```

```python
import jax
import jax.numpy as jnp
from jax import lax
from jax.experimental import pallas as pl
from jax.experimental.pallas import tpu as pltpu
from jax.sharding import PartitionSpec as P

CAP = 2
BAND = 2
RBLK = 32


def split_bf16(values):
    high = values.astype(jnp.bfloat16)
    low = (values - high.astype(jnp.float32)).astype(jnp.bfloat16)
    return high, low


def tile_kernel(weight_ref, exchange_ref, basis_t_ref, basis_ref, inner_t_ref, out_ref, lhs_ref, rhs_ref):
    point_count = basis_ref.shape[0]
    lhs_ref[:, point_count:] = inner_t_ref[...]
    rhs_ref[:point_count, :] = basis_ref[...]
    basis_t = basis_t_ref[...]
    for j in range(out_ref.shape[0]):
        lhs_ref[:, :point_count] = (basis_t * weight_ref[j : j + 1, :]).astype(jnp.bfloat16)
        rhs_ref[point_count:, :] = exchange_ref[j]
        acc = jnp.dot(lhs_ref[...], rhs_ref[...], preferred_element_type=jnp.float32)
        out_ref[j] = acc.astype(out_ref.dtype)


def build_blocks(weight_sum, exchange_sum, basis, group=32):
    block_count, point_count = weight_sum.shape
    inner_count, spline_count = exchange_sum.shape[1:]
    basis_t = basis.T.astype(jnp.float32)
    inner_t = basis[:inner_count].T
    depth = point_count + inner_count
    return pl.pallas_call(
        tile_kernel,
        grid=(block_count // group,),
        in_specs=[
            pl.BlockSpec((group, point_count), lambda g: (g, 0)),
            pl.BlockSpec((group, inner_count, spline_count), lambda g: (g, 0, 0)),
            pl.BlockSpec((spline_count, point_count), lambda g: (0, 0)),
            pl.BlockSpec((point_count, spline_count), lambda g: (0, 0)),
            pl.BlockSpec((spline_count, inner_count), lambda g: (0, 0)),
        ],
        out_specs=pl.BlockSpec((group, spline_count, spline_count), lambda g: (g, 0, 0)),
        out_shape=jax.ShapeDtypeStruct((block_count, spline_count, spline_count), jnp.bfloat16),
        scratch_shapes=[
            pltpu.VMEM((spline_count, depth), jnp.bfloat16),
            pltpu.VMEM((depth, spline_count), jnp.bfloat16),
        ],
    )(weight_sum, exchange_sum, basis_t, basis, inner_t)


def on_device(basis, potentials, orbitals, chan_orbital, pair_list, slot_list, coefs, exchange_ops):
    row_devs = lax.axis_size("prow")
    col_devs = lax.axis_size("pcol")
    slot_count = row_devs * col_devs * CAP
    chan_count = chan_orbital.shape[0]
    point_count = basis.shape[0]
    spline_count = basis.shape[1]
    inner_count = exchange_ops.shape[1]
    col_groups = chan_count // col_devs
    block_count = RBLK * BAND
    first_chan = pair_list[:, 0]
    second_chan = pair_list[:, 1]
    multipole = pair_list[:, 2]
    matches = slot_list[None, :] == jnp.arange(slot_count, dtype=jnp.int32)[:, None]

    slot_exchange = jnp.einsum(
        "st,tqb->sqb",
        matches.astype(jnp.bfloat16),
        exchange_ops,
        preferred_element_type=jnp.float32,
    ).astype(jnp.bfloat16)
    received_exchange = lax.all_to_all(slot_exchange, ("prow", "pcol"), 0, 0, tiled=True)

    channels = jnp.arange(chan_count, dtype=jnp.int32)
    first_orb = jnp.sum(
        jnp.where(first_chan[:, None] == channels[None, :], chan_orbital[None, :], 0), axis=1
    )
    second_orb = jnp.sum(
        jnp.where(second_chan[:, None] == channels[None, :], chan_orbital[None, :], 0), axis=1
    )
    match_float = matches.astype(jnp.float32)
    pick_pot = (
        multipole[:, None] == jnp.arange(potentials.shape[0], dtype=jnp.int32)[None, :]
    ).astype(jnp.float32)
    slot_pot_coef = jnp.dot(
        match_float * coefs[None, :, 0], pick_pot, precision=lax.Precision.HIGHEST
    )
    slot_pot = jnp.dot(slot_pot_coef, potentials, precision=lax.Precision.HIGHEST)
    slot_orb_coef = jnp.dot(match_float, coefs[:, 1], precision=lax.Precision.HIGHEST)
    offset = jnp.mod(second_chan // col_devs - first_chan // col_devs, col_groups)
    block_index = first_chan // row_devs * BAND + offset

    def per_slot(values):
        return jnp.max(jnp.where(matches, values[None, :], -1), axis=1).astype(jnp.float32)

    tail = jnp.stack(
        [slot_orb_coef, per_slot(first_orb), per_slot(second_orb), per_slot(block_index)], axis=1
    )
    width = -(-(point_count + tail.shape[1]) // 128) * 128
    small = jnp.concatenate(
        [
            slot_pot,
            tail,
            jnp.zeros((slot_count, width - point_count - tail.shape[1]), jnp.float32),
        ],
        axis=1,
    )
    received_small = lax.all_to_all(small, ("prow", "pcol"), 0, 0, tiled=True)

    all_orbitals = lax.all_gather(orbitals, "pcol", axis=0, tiled=True)
    orb_ids = jnp.arange(all_orbitals.shape[0], dtype=jnp.int32)
    recv_first = received_small[:, point_count + 1].astype(jnp.int32)
    recv_second = received_small[:, point_count + 2].astype(jnp.int32)
    idents = received_small[:, point_count + 3].astype(jnp.int32)
    first_rows = jnp.dot(
        (recv_first[:, None] == orb_ids[None, :]).astype(jnp.bfloat16),
        all_orbitals,
        preferred_element_type=jnp.float32,
    )
    second_rows = jnp.dot(
        (recv_second[:, None] == orb_ids[None, :]).astype(jnp.bfloat16),
        all_orbitals,
        preferred_element_type=jnp.float32,
    )
    slot_weight = (
        received_small[:, :point_count]
        + received_small[:, point_count : point_count + 1] * (first_rows * second_rows)
    ).astype(jnp.bfloat16)

    select = (jnp.arange(block_count, dtype=jnp.int32)[:, None] == idents[None, :]).astype(
        jnp.bfloat16
    )
    weight_sum = jnp.dot(select, slot_weight, preferred_element_type=jnp.float32)
    exchange_sum = jnp.einsum(
        "gs,sqb->gqb", select, received_exchange, preferred_element_type=jnp.float32
    ).astype(jnp.bfloat16)
    blocks = build_blocks(weight_sum, exchange_sum, basis)
    return blocks.reshape(RBLK, 1, BAND, 1, spline_count, spline_count)


def solution(mesh):
    placed = (
        P(),
        P(),
        P("pcol", None),
        P(),
        P(("prow", "pcol"), None),
        P(("prow", "pcol")),
        P(("prow", "pcol"), None),
        P(("prow", "pcol"), None, None),
    )
    return jax.shard_map(
        on_device,
        mesh=mesh,
        in_specs=placed,
        out_specs=P(None, "prow", None, "pcol", None, None),
        check_vma=False,
    )
```
